256 devices in a mesh: lev: 32 (over y_hi, z, core), pln: 8 (over y_lo, x).
Axes of the slice: x: 4, y: 4 (y_hi: 2, y_lo: 2; y = y_hi * 2 + y_lo), z: 8, core: 2. Of those that a mesh axis runs over, the one named last changes fastest.
Arguments:
- concentration: float32 [128, 1024, 1024], P('lev', 'pln'), may hold values from -2.5 to 2.5
- potential: float32 [1024, 1024], P('pln'), may hold values from -1.5 to 1.5
- lift: float32 [128], replicated, may hold values from 1 to 8
- eigenvalue: float32 [128], replicated, may hold values from 0.05 to 20
- basis: float32 [128, 128], replicated, may hold values from -1 to 2, as said below
- inverse_basis: float32 [128, 128], replicated, may hold values from -1 to 2, as said below
Outputs:
- next_concentration: float32 [128, 1024, 1024], P('lev', 'pln')
The draws below stay inside these ranges and needn't reach their ends.
Inputs may be any that keep to these rules, and one draw needn't show every extreme that they name: basis times inverse_basis is the identity up to float32 rounding. `inverse_basis`: the matrix inverse of basis, up to float32 rounding.
All inputs are finite; a program needn't handle non-finite values.
Results may differ from the reference program's by a relative error of at most 0.00035.
Values sent between devices are 32-bit elements; how exact they have to be, the bound alone decides.
No kernel may reach another device: no remote copies, remote signals or barrier semaphores. Data moves between devices by JAX's collectives and lax.ppermute only.
A program may use at most 128 MiB of HBM per device.

```python
import math
import jax
import jax.numpy as jnp
from jax import lax

NX = 1024
NY = 1024
LEVELS = 128


def draw_concentration(key, part):
    return 0.5 * jax.random.truncated_normal(key, -5.0, 5.0, (LEVELS, NX, NY), jnp.float32)


def basis_pair(key):
    own_key = jax.random.fold_in(key, 11)
    spread = 0.35 / jnp.sqrt(jnp.float32(LEVELS))
    offdiag = jax.random.truncated_normal(own_key, -4.0, 4.0, (LEVELS, LEVELS), jnp.float32) * spread
    matrix = jnp.eye(LEVELS, dtype=jnp.float32) + offdiag
    return (matrix, jnp.linalg.inv(matrix))


def draw_basis(key, part):
    return basis_pair(key)[0]


def draw_inverse_basis(key, part):
    return basis_pair(key)[1]


def shard_levels(rng, dims, cuts, smallest, top_value):
    gain = 1.0
    for dim, parts in cuts:
        draws = jax.random.uniform(jax.random.fold_in(jax.random.fold_in(rng, 6), dim), (parts,), jnp.float32, smallest / len(cuts), top_value / len(cuts))
        gain = gain * jnp.repeat(jnp.exp(draws), dims[dim] // parts).reshape((-1,) + (1,) * (len(dims) - 1 - dim))
    return gain


def setup_inputs(seed: int = 0) -> dict:
    seeds = jax.random.split(jax.random.key(seed), 7)
    concentration = draw_concentration(jax.random.fold_in(seeds[6], 71), 0)
    potential = jnp.clip(jax.random.uniform(seeds[1], (NX, NY), jnp.float32, -1.5, 1.5) * shard_levels(seeds[1], (NX, NY), ((0, 8),), -0.4, 0.0), -1.5, 1.5)
    lift = jnp.clip(jnp.exp(jax.random.uniform(seeds[2], (LEVELS,), jnp.float32, math.log(1.0), math.log(8.0))), 1.0, 8.0)
    eigenvalue = jnp.clip(jnp.exp(jax.random.uniform(seeds[3], (LEVELS,), jnp.float32, math.log(0.05), math.log(20.0))), 0.05, 20.0)
    basis = draw_basis(jax.random.fold_in(seeds[6], 71), 0)
    inverse_basis = draw_inverse_basis(jax.random.fold_in(seeds[6], 71), 0)
    return dict(concentration=concentration, potential=potential, lift=lift, eigenvalue=eigenvalue, basis=basis, inverse_basis=inverse_basis)


TIME_STEP = 0.04
GRADIENT_ENERGY = 0.25
EXCHANGE_CURRENT = 0.6

def cas_transform(field, axis):
    spectrum = jnp.fft.fft(field, axis=axis)
    return spectrum.real - spectrum.imag

def wave_squared(length):
    index = jnp.arange(length, dtype=jnp.int32)
    folded = jnp.minimum(index, length - index).astype(jnp.float32)
    return (folded * (2.0 * jnp.pi / length)) ** 2

def reference(concentration, potential, lift, eigenvalue, basis, inverse_basis):
    highest = lax.Precision.HIGHEST
    surface = 2.0 * EXCHANGE_CURRENT * jnp.sinh(0.5 * (potential - concentration[0]))
    shifted = concentration + TIME_STEP * lift[:, None, None] * surface[None]
    nonlinear = concentration ** 3 - concentration

    def forward(planes):
        return (cas_transform(cas_transform(planes[0], 1), 0), cas_transform(cas_transform(planes[1], 1), 0))
    first_modes, second_modes = lax.map(forward, (shifted, nonlinear))
    eigen_first = jnp.einsum('ml,lxy->mxy', inverse_basis, first_modes, precision=highest)
    eigen_second = jnp.einsum('ml,lxy->mxy', inverse_basis, second_modes, precision=highest)
    total_wave = wave_squared(NX)[:, None] + wave_squared(NY)[None, :]
    operator = total_wave[None] + eigenvalue[:, None, None]
    update = (eigen_first - TIME_STEP * operator * eigen_second) / (1.0 + TIME_STEP * GRADIENT_ENERGY * operator * operator)
    level_values = jnp.einsum('lm,mxy->lxy', basis, update, precision=highest)

    def backward(plane):
        return cas_transform(cas_transform(plane, 1), 0) * (1.0 / (NX * NY))
    return lax.map(backward, level_values)
```

```python
import math

import jax
import jax.numpy as jnp
from jax import lax
from jax.sharding import PartitionSpec as P

TIME_STEP = 0.04
GRADIENT_ENERGY = 0.25
EXCHANGE_CURRENT = 0.6


def cas_table(length):
    index = jnp.arange(length, dtype=jnp.int32)
    product = index[:, None] * index[None, :] % length
    angle = product.astype(jnp.float32) * (2.0 * jnp.pi / length)
    return math.sqrt(2.0) * jnp.sin(angle + 0.25 * jnp.pi)


def wave_squared(index, length):
    folded = jnp.minimum(index, length - index).astype(jnp.float32)
    return (folded * (2.0 * jnp.pi / length)) ** 2


def body(concentration, potential, lift, eigenvalue, basis, inverse_basis):
    highest = lax.Precision.HIGHEST
    fast = lax.Precision.HIGH
    lev_count = lax.axis_size("lev")
    pln_count = lax.axis_size("pln")
    lev_index = lax.axis_index("lev")
    pln_index = lax.axis_index("pln")
    own_levels, own_rows, width_y = concentration.shape
    width_x = own_rows * pln_count
    cols_y = width_y // pln_count
    rows_x = width_x // lev_count
    table_y = lax.optimization_barrier(cas_table(width_y))
    table_x = table_y if width_x == width_y else lax.optimization_barrier(cas_table(width_x))
    nonlinear = concentration**3 - concentration
    surface = 2.0 * EXCHANGE_CURRENT * jnp.sinh(0.5 * (potential - concentration[0]))
    stacked = jnp.concatenate([concentration, nonlinear, surface[None]], axis=0)
    along_y = jnp.einsum("lxn,nk->lxk", stacked, table_y, precision=fast)
    spectral = jnp.einsum(
        "kx,lxj->lkj",
        table_x,
        lax.all_to_all(along_y, "pln", split_axis=2, concat_axis=1, tiled=True),
        precision=fast,
    )
    first_modes = jnp.concatenate([spectral[:own_levels], spectral[2 * own_levels :]], axis=0)
    second_modes = spectral[own_levels : 2 * own_levels]
    gathered_first = lax.all_to_all(first_modes, "lev", split_axis=1, concat_axis=0, tiled=True)
    gathered_second = lax.all_to_all(second_modes, "lev", split_axis=1, concat_axis=0, tiled=True)
    gathered_first = gathered_first.reshape(lev_count, own_levels + 1, rows_x, cols_y)
    conc_modes = gathered_first[:, :own_levels].reshape(lev_count * own_levels, rows_x, cols_y)
    surface_modes = gathered_first[0, own_levels]
    lift_weight = jnp.einsum("ml,l->m", inverse_basis, lift, precision=highest)
    eigen_first = (
        jnp.einsum("ml,lxy->mxy", inverse_basis, conc_modes, precision=highest)
        + TIME_STEP * lift_weight[:, None, None] * surface_modes[None]
    )
    eigen_second = jnp.einsum("ml,lxy->mxy", inverse_basis, gathered_second, precision=highest)
    x_index = lev_index * rows_x + jnp.arange(rows_x, dtype=jnp.int32)
    y_index = pln_index * cols_y + jnp.arange(cols_y, dtype=jnp.int32)
    total_wave = wave_squared(x_index, width_x)[:, None] + wave_squared(y_index, width_y)[None, :]
    operator = total_wave[None] + eigenvalue[:, None, None]
    numerator = eigen_first - TIME_STEP * operator * eigen_second
    update = numerator / (1.0 + TIME_STEP * GRADIENT_ENERGY * operator * operator)
    level_values = jnp.einsum("lm,mxy->lxy", basis, update, precision=highest)
    returned = lax.all_to_all(level_values, "lev", split_axis=0, concat_axis=1, tiled=True)
    back_x = jnp.einsum("kx,lxj->lkj", table_x, returned, precision=fast)
    scale_factor = 1.0 / (width_x * width_y)
    return (
        jnp.einsum(
            "lxn,nk->lxk",
            lax.all_to_all(back_x, "pln", split_axis=1, concat_axis=2, tiled=True),
            table_y,
            precision=fast,
        )
        * scale_factor
    )


def solution(mesh):
    in_specs = (P("lev", "pln", None), P("pln", None), P(), P(), P(), P())
    out_specs = P("lev", "pln", None)
    return jax.shard_map(body, mesh=mesh, in_specs=in_specs, out_specs=out_specs, check_vma=False)
```

```python
import math

import jax
import jax.numpy as jnp
from jax import lax
from jax.sharding import PartitionSpec as P

TIME_STEP = 0.04
GRADIENT_ENERGY = 0.25
EXCHANGE_CURRENT = 0.6


def unit_phase(numerator, denominator):
    angle = numerator.astype(jnp.float32) * (2.0 * jnp.pi / denominator)
    return jnp.cos(angle), jnp.sin(angle)


def cas_table(length):
    b = 1 << (int(math.log2(length)) // 2)
    if length % b:
        index = jnp.arange(length, dtype=jnp.int32)
        cos_part, sin_part = unit_phase(index[:, None] * index[None, :] % length, length)
        return cos_part + sin_part
    a = length // b
    k1 = jnp.arange(a, dtype=jnp.int32)[:, None, None, None]
    k0 = jnp.arange(b, dtype=jnp.int32)[None, :, None, None]
    m1 = jnp.arange(b, dtype=jnp.int32)[None, None, :, None]
    m0 = jnp.arange(a, dtype=jnp.int32)[None, None, None, :]
    ar, ai = unit_phase(k1 * m0 % a, a)
    br, bi = unit_phase(k0 * m1 % b, b)
    cr, ci = unit_phase(k0 * m0, length)
    dr = ar * br - ai * bi
    di = ar * bi + ai * br
    table = dr * (cr + ci) + di * (cr - ci)
    return table.reshape(length, length)


def wave_squared(index, length):
    folded = jnp.minimum(index, length - index).astype(jnp.float32)
    return (folded * (2.0 * jnp.pi / length)) ** 2


def body(concentration, potential, lift, eigenvalue, basis, inverse_basis):
    highest = lax.Precision.HIGHEST
    fast = lax.Precision.HIGH
    lev_count = lax.axis_size("lev")
    pln_count = lax.axis_size("pln")
    lev_index = lax.axis_index("lev")
    pln_index = lax.axis_index("pln")
    own_levels, own_rows, width_y = concentration.shape
    width_x = own_rows * pln_count
    cols_y = width_y // pln_count
    rows_x = width_x // lev_count
    table_y = lax.optimization_barrier(cas_table(width_y))
    table_x = table_y if width_x == width_y else lax.optimization_barrier(cas_table(width_x))
    nonlinear = concentration**3 - concentration
    surface = 2.0 * EXCHANGE_CURRENT * jnp.sinh(0.5 * (potential - concentration[0]))
    stacked = jnp.concatenate([concentration, surface[None], nonlinear], axis=0)
    planes = stacked.shape[0]
    along_y = jnp.einsum("lxn,nk->lxk", stacked, table_y, precision=fast)
    send_p = along_y.reshape(planes, own_rows, pln_count, cols_y).transpose(2, 0, 1, 3)
    recv_p = lax.all_to_all(send_p, "pln", split_axis=0, concat_axis=0, tiled=True)
    table_fx = table_x.reshape(lev_count, rows_x, pln_count, own_rows)
    spectral = jnp.einsum("dksx,slxj->dlkj", table_fx, recv_p, precision=fast)
    gathered = lax.all_to_all(spectral, "lev", split_axis=0, concat_axis=0, tiled=True)
    basis_inv = inverse_basis.reshape(inverse_basis.shape[0], lev_count, own_levels)
    lift_weight = jnp.einsum("ml,l->m", inverse_basis, lift, precision=highest)
    eigen_first = (
        jnp.einsum("msi,sikj->mkj", basis_inv, gathered[:, :own_levels], precision=highest)
        + TIME_STEP * lift_weight[:, None, None] * gathered[0, own_levels][None]
    )
    eigen_second = jnp.einsum("msi,sikj->mkj", basis_inv, gathered[:, own_levels + 1 :], precision=highest)
    x_index = lev_index * rows_x + jnp.arange(rows_x, dtype=jnp.int32)
    y_index = pln_index * cols_y + jnp.arange(cols_y, dtype=jnp.int32)
    total_wave = wave_squared(x_index, width_x)[:, None] + wave_squared(y_index, width_y)[None, :]
    operator = total_wave[None] + eigenvalue[:, None, None]
    numerator = eigen_first - TIME_STEP * operator * eigen_second
    update = numerator / (1.0 + TIME_STEP * GRADIENT_ENERGY * operator * operator)
    level_values = jnp.einsum("lm,mxy->lxy", basis, update, precision=highest)
    send_l = level_values.reshape(lev_count, own_levels, rows_x, cols_y)
    returned = lax.all_to_all(send_l, "lev", split_axis=0, concat_axis=0, tiled=True)
    table_bx = table_x.reshape(pln_count, own_rows, lev_count, rows_x)
    back_x = jnp.einsum("dxsk,slkj->dlxj", table_bx, returned, precision=fast)
    back_p = lax.all_to_all(back_x, "pln", split_axis=0, concat_axis=0, tiled=True)
    table_by = table_y.reshape(pln_count, cols_y, width_y)
    scale_factor = 1.0 / (width_x * width_y)
    return jnp.einsum("slxj,sjn->lxn", back_p, table_by, precision=fast) * scale_factor


def solution(mesh):
    in_specs = (P("lev", "pln", None), P("pln", None), P(), P(), P(), P())
    out_specs = P("lev", "pln", None)
    return jax.shard_map(body, mesh=mesh, in_specs=in_specs, out_specs=out_specs, check_vma=False)
```

```python
import math

import jax
import jax.numpy as jnp
from jax import lax
from jax.sharding import PartitionSpec as P

TIME_STEP = 0.04
GRADIENT_ENERGY = 0.25
EXCHANGE_CURRENT = 0.6


def unit_phase(numerator, denominator):
    angle = numerator.astype(jnp.float32) * (2.0 * jnp.pi / denominator)
    return lax.optimization_barrier((jnp.cos(angle), jnp.sin(angle)))


def cas_table(length):
    b = 1 << (int(math.log2(length)) // 2)
    if length % b:
        index = jnp.arange(length, dtype=jnp.int32)
        cos_part, sin_part = unit_phase(index[:, None] * index[None, :] % length, length)
        return cos_part + sin_part
    a = length // b
    k1 = jnp.arange(a, dtype=jnp.int32)[:, None, None, None]
    k0 = jnp.arange(b, dtype=jnp.int32)[None, :, None, None]
    m1 = jnp.arange(b, dtype=jnp.int32)[None, None, :, None]
    m0 = jnp.arange(a, dtype=jnp.int32)[None, None, None, :]
    ar, ai = unit_phase(k1 * m0 % a, a)
    br, bi = unit_phase(k0 * m1 % b, b)
    cr, ci = unit_phase(k0 * m0, length)
    dr = ar * br - ai * bi
    di = ar * bi + ai * br
    table = dr * (cr + ci) + di * (cr - ci)
    return table.reshape(length, length)


def wave_squared(index, length):
    folded = jnp.minimum(index, length - index).astype(jnp.float32)
    return (folded * (2.0 * jnp.pi / length)) ** 2


def body(concentration, potential, lift, eigenvalue, basis, inverse_basis):
    highest = lax.Precision.HIGHEST
    fast = lax.Precision.HIGH
    both = ("lev", "pln")
    lev_count = lax.axis_size("lev")
    pln_count = lax.axis_size("pln")
    devices = lev_count * pln_count
    flat_index = lax.axis_index("lev") * pln_count + lax.axis_index("pln")
    own_levels, own_rows, width_y = concentration.shape
    width_x = own_rows * pln_count
    cols = width_y // devices
    table_y = lax.optimization_barrier(cas_table(width_y))
    table_x = table_y if width_x == width_y else lax.optimization_barrier(cas_table(width_x))
    nonlinear = concentration**3 - concentration
    surface = 2.0 * EXCHANGE_CURRENT * jnp.sinh(0.5 * (potential - concentration[0]))
    stacked = jnp.concatenate([concentration, surface[None], nonlinear], axis=0)
    planes = stacked.shape[0]
    along_y = jnp.einsum("lxn,nk->lkx", stacked, table_y, precision=fast)
    send = along_y.reshape(planes, devices, cols, own_rows).transpose(1, 0, 2, 3)
    send = send.reshape(devices, planes * cols, own_rows)
    recv = lax.all_to_all(send, both, split_axis=0, concat_axis=0, tiled=True)
    recv = recv.reshape(lev_count, pln_count, planes, cols, own_rows)
    table_rx = table_x.reshape(pln_count, own_rows, width_x)
    spectral = jnp.einsum("aplkx,pxn->alkn", recv, table_rx, precision=fast)
    basis_inv = inverse_basis.reshape(inverse_basis.shape[0], lev_count, own_levels)
    lift_weight = jnp.einsum("ml,l->m", inverse_basis, lift, precision=highest)
    eigen_first = (
        jnp.einsum("mai,aikn->mkn", basis_inv, spectral[:, :own_levels], precision=highest)
        + TIME_STEP * lift_weight[:, None, None] * spectral[0, own_levels][None]
    )
    eigen_second = jnp.einsum("mai,aikn->mkn", basis_inv, spectral[:, own_levels + 1 :], precision=highest)
    y_index = flat_index * cols + jnp.arange(cols, dtype=jnp.int32)
    x_index = jnp.arange(width_x, dtype=jnp.int32)
    total_wave = wave_squared(y_index, width_y)[:, None] + wave_squared(x_index, width_x)[None, :]
    operator = total_wave[None] + eigenvalue[:, None, None]
    numerator = eigen_first - TIME_STEP * operator * eigen_second
    update = numerator / (1.0 + TIME_STEP * GRADIENT_ENERGY * operator * operator)
    level_values = jnp.einsum("lm,mkn->lkn", basis, update, precision=highest)
    back_x = jnp.einsum("lkn,nx->lkx", level_values, table_x, precision=fast)
    send_b = back_x.reshape(lev_count, own_levels, cols, pln_count, own_rows).transpose(0, 3, 1, 2, 4)
    send_b = send_b.reshape(devices, own_levels * cols, own_rows)
    recv_b = lax.all_to_all(send_b, both, split_axis=0, concat_axis=0, tiled=True)
    recv_b = recv_b.reshape(devices, own_levels, cols, own_rows)
    table_by = table_y.reshape(devices, cols, width_y)
    scale_factor = 1.0 / (width_x * width_y)
    return jnp.einsum("qijx,qjn->ixn", recv_b, table_by, precision=fast) * scale_factor


def solution(mesh):
    in_specs = (P("lev", "pln", None), P("pln", None), P(), P(), P(), P())
    out_specs = P("lev", "pln", None)
    return jax.shard_map(body, mesh=mesh, in_specs=in_specs, out_specs=out_specs, check_vma=False)
```

```python
import math

import jax
import jax.numpy as jnp
from jax import lax
from jax.sharding import PartitionSpec as P

TIME_STEP = 0.04
GRADIENT_ENERGY = 0.25
EXCHANGE_CURRENT = 0.6


def unit_phase(numerator, denominator):
    angle = numerator.astype(jnp.float32) * (2.0 * jnp.pi / denominator)
    return lax.optimization_barrier((jnp.cos(angle), jnp.sin(angle)))


def cas_table(length):
    b = 1 << (int(math.log2(length)) // 2)
    if length % b:
        index = jnp.arange(length, dtype=jnp.int32)
        cos_part, sin_part = unit_phase(index[:, None] * index[None, :] % length, length)
        return cos_part + sin_part
    a = length // b
    m = jnp.arange(length, dtype=jnp.int32)[None, :]
    m1 = m // a
    m0 = m % a
    k1 = jnp.arange(a, dtype=jnp.int32)[:, None]
    k0 = jnp.arange(b, dtype=jnp.int32)[:, None]
    ar, ai = unit_phase(k1 * m0 % a, a)
    br, bi = unit_phase(k0 * m1 % b, b)
    cr, ci = unit_phase(k0 * m0, length)
    er = br * cr - bi * ci
    ei = br * ci + bi * cr
    plus, minus = lax.optimization_barrier((er + ei, er - ei))
    table = ar[:, None, :] * plus[None] + ai[:, None, :] * minus[None]
    return table.reshape(length, length)


def wave_squared(index, length):
    folded = jnp.minimum(index, length - index).astype(jnp.float32)
    return (folded * (2.0 * jnp.pi / length)) ** 2


def body(concentration, potential, lift, eigenvalue, basis, inverse_basis):
    highest = lax.Precision.HIGHEST
    fast = lax.Precision.HIGH
    both = ("lev", "pln")
    lev_count = lax.axis_size("lev")
    pln_count = lax.axis_size("pln")
    devices = lev_count * pln_count
    flat_index = lax.axis_index("lev") * pln_count + lax.axis_index("pln")
    own_levels, own_rows, width_y = concentration.shape
    width_x = own_rows * pln_count
    cols = width_y // devices
    table_y = lax.optimization_barrier(cas_table(width_y))
    table_x = table_y if width_x == width_y else lax.optimization_barrier(cas_table(width_x))
    nonlinear = concentration**3 - concentration
    surface = 2.0 * EXCHANGE_CURRENT * jnp.sinh(0.5 * (potential - concentration[0]))
    stacked = jnp.concatenate([concentration, surface[None], nonlinear], axis=0)
    planes = stacked.shape[0]
    along_y = lax.optimization_barrier(jnp.einsum("lxn,nk->lxk", stacked, table_y, precision=fast))
    send = along_y.reshape(planes, own_rows, devices, cols).transpose(2, 0, 3, 1)
    send = send.reshape(devices, planes * cols, own_rows)
    recv = lax.all_to_all(send, both, split_axis=0, concat_axis=0, tiled=True)
    recv = recv.reshape(lev_count, pln_count, planes, cols, own_rows)
    table_rx = table_x.reshape(pln_count, own_rows, width_x)
    spectral = jnp.einsum("aplkx,pxn->alkn", recv, table_rx, precision=fast)
    basis_inv = inverse_basis.reshape(inverse_basis.shape[0], lev_count, own_levels)
    lift_weight = jnp.einsum("ml,l->m", inverse_basis, lift, precision=highest)
    eigen_first = (
        jnp.einsum("mai,aikn->mkn", basis_inv, spectral[:, :own_levels], precision=highest)
        + TIME_STEP * lift_weight[:, None, None] * spectral[0, own_levels][None]
    )
    eigen_second = jnp.einsum("mai,aikn->mkn", basis_inv, spectral[:, own_levels + 1 :], precision=highest)
    y_index = flat_index * cols + jnp.arange(cols, dtype=jnp.int32)
    x_index = jnp.arange(width_x, dtype=jnp.int32)
    total_wave = wave_squared(y_index, width_y)[:, None] + wave_squared(x_index, width_x)[None, :]
    operator = total_wave[None] + eigenvalue[:, None, None]
    numerator = eigen_first - TIME_STEP * operator * eigen_second
    update = numerator / (1.0 + TIME_STEP * GRADIENT_ENERGY * operator * operator)
    level_values = jnp.einsum("lm,mkn->lkn", basis, update, precision=highest)
    back_x = jnp.einsum("lkn,nx->lkx", level_values, table_x, precision=fast)
    send_b = back_x.reshape(lev_count, own_levels, cols, pln_count, own_rows).transpose(0, 3, 1, 2, 4)
    send_b = send_b.reshape(devices, own_levels * cols, own_rows)
    recv_b = lax.all_to_all(send_b, both, split_axis=0, concat_axis=0, tiled=True)
    recv_b = recv_b.reshape(devices, own_levels, cols, own_rows).transpose(1, 3, 0, 2)
    recv_b = lax.optimization_barrier(recv_b.reshape(own_levels, own_rows, width_y))
    scale_factor = 1.0 / (width_x * width_y)
    return jnp.einsum("ixk,kn->ixn", recv_b, table_y, precision=fast) * scale_factor


def solution(mesh):
    in_specs = (P("lev", "pln", None), P("pln", None), P(), P(), P(), P())
    out_specs = P("lev", "pln", None)
    return jax.shard_map(body, mesh=mesh, in_specs=in_specs, out_specs=out_specs, check_vma=False)
```

```python
import math

import jax
import jax.numpy as jnp
from jax import lax
from jax.sharding import PartitionSpec as P

TIME_STEP = 0.04
GRADIENT_ENERGY = 0.25
EXCHANGE_CURRENT = 0.6


def unit_phase(numerator, denominator):
    angle = numerator.astype(jnp.float32) * (2.0 * jnp.pi / denominator)
    return lax.optimization_barrier((jnp.cos(angle), jnp.sin(angle)))


def cas_table(length):
    b = 1 << (int(math.log2(length)) // 2)
    if length % b:
        index = jnp.arange(length, dtype=jnp.int32)
        cos_part, sin_part = unit_phase(index[:, None] * index[None, :] % length, length)
        return cos_part + sin_part
    a = length // b
    m = jnp.arange(length, dtype=jnp.int32)[None, :]
    m1 = m // a
    m0 = m % a
    k1 = jnp.arange(a, dtype=jnp.int32)[:, None]
    k0 = jnp.arange(b, dtype=jnp.int32)[:, None]
    ar, ai = unit_phase(k1 * m0 % a, a)
    br, bi = unit_phase(k0 * m1 % b, b)
    cr, ci = unit_phase(k0 * m0, length)
    er = br * cr - bi * ci
    ei = br * ci + bi * cr
    plus, minus = lax.optimization_barrier((er + ei, er - ei))
    table = ar[:, None, :] * plus[None] + ai[:, None, :] * minus[None]
    return table.reshape(length, length)


def wave_squared(index, length):
    folded = jnp.minimum(index, length - index).astype(jnp.float32)
    return (folded * (2.0 * jnp.pi / length)) ** 2


def body(concentration, potential, lift, eigenvalue, basis, inverse_basis):
    fast = lax.Precision.HIGH
    both = ("lev", "pln")
    lev_count = lax.axis_size("lev")
    pln_count = lax.axis_size("pln")
    devices = lev_count * pln_count
    flat_index = lax.axis_index("lev") * pln_count + lax.axis_index("pln")
    own_levels, own_rows, width_y = concentration.shape
    width_x = own_rows * pln_count
    cols = width_y // devices
    table_y = lax.optimization_barrier(cas_table(width_y))
    table_x = table_y if width_x == width_y else lax.optimization_barrier(cas_table(width_x))
    table_rx = table_x.reshape(pln_count, own_rows, width_x)

    def forward(planes_in):
        planes = planes_in.shape[0]
        along_y = lax.optimization_barrier(jnp.einsum("lxn,nk->lxk", planes_in, table_y, precision=fast))
        send = along_y.reshape(planes, own_rows, devices, cols).transpose(2, 0, 3, 1)
        send = send.reshape(devices, planes * cols, own_rows)
        recv = lax.all_to_all(send, both, split_axis=0, concat_axis=0, tiled=True)
        recv = recv.reshape(lev_count, pln_count, planes, cols, own_rows)
        return jnp.einsum("aplkx,pxn->alkn", recv, table_rx, precision=fast)

    nonlinear = concentration**3 - concentration
    surface = 2.0 * EXCHANGE_CURRENT * jnp.sinh(0.5 * (potential - concentration[0]))
    first_spectral = forward(jnp.concatenate([concentration, surface[None]], axis=0))
    second_spectral = forward(nonlinear)
    basis_inv = inverse_basis.reshape(inverse_basis.shape[0], lev_count, own_levels)
    lift_weight = jnp.einsum("ml,l->m", inverse_basis, lift, precision=lax.Precision.HIGHEST)
    eigen_first = (
        jnp.einsum("mai,aikn->mkn", basis_inv, first_spectral[:, :own_levels], precision=fast)
        + TIME_STEP * lift_weight[:, None, None] * first_spectral[0, own_levels][None]
    )
    eigen_second = jnp.einsum("mai,aikn->mkn", basis_inv, second_spectral, precision=fast)
    y_index = flat_index * cols + jnp.arange(cols, dtype=jnp.int32)
    x_index = jnp.arange(width_x, dtype=jnp.int32)
    total_wave = wave_squared(y_index, width_y)[:, None] + wave_squared(x_index, width_x)[None, :]
    operator = total_wave[None] + eigenvalue[:, None, None]
    numerator = eigen_first - TIME_STEP * operator * eigen_second
    update = numerator / (1.0 + TIME_STEP * GRADIENT_ENERGY * operator * operator)
    basis_rows = basis.reshape(lev_count, own_levels, basis.shape[1])
    scale_factor = 1.0 / (width_x * width_y)
    half = own_levels // 2 if own_levels % 2 == 0 else own_levels
    outputs = []
    for first_level in range(0, own_levels, half):
        chunk = basis_rows[:, first_level : first_level + half]
        level_values = jnp.einsum("aim,mkn->aikn", chunk, update, precision=fast)
        back_x = jnp.einsum("aikn,nx->aikx", level_values, table_x, precision=fast)
        send_b = back_x.reshape(lev_count, half, cols, pln_count, own_rows).transpose(0, 3, 1, 2, 4)
        send_b = send_b.reshape(devices, half * cols, own_rows)
        recv_b = lax.all_to_all(send_b, both, split_axis=0, concat_axis=0, tiled=True)
        recv_b = recv_b.reshape(devices, half, cols, own_rows).transpose(1, 3, 0, 2)
        recv_b = lax.optimization_barrier(recv_b.reshape(half, own_rows, width_y))
        outputs.append(jnp.einsum("ixk,kn->ixn", recv_b, table_y, precision=fast) * scale_factor)
    return jnp.concatenate(outputs, axis=0)


def solution(mesh):
    in_specs = (P("lev", "pln", None), P("pln", None), P(), P(), P(), P())
    out_specs = P("lev", "pln", None)
    return jax.shard_map(body, mesh=mesh, in_specs=in_specs, out_specs=out_specs, check_vma=False)
```

```python
import math

import jax
import jax.numpy as jnp
from jax import lax
from jax.sharding import PartitionSpec as P

TIME_STEP = 0.04
GRADIENT_ENERGY = 0.25
EXCHANGE_CURRENT = 0.6


def unit_phase(numerator, denominator):
    angle = numerator.astype(jnp.float32) * (2.0 * jnp.pi / denominator)
    return lax.optimization_barrier((jnp.cos(angle), jnp.sin(angle)))


def cas_table(length):
    b = 1 << (int(math.log2(length)) // 2)
    if length % b:
        index = jnp.arange(length, dtype=jnp.int32)
        cos_part, sin_part = unit_phase(index[:, None] * index[None, :] % length, length)
        return cos_part + sin_part
    a = length // b
    m = jnp.arange(length, dtype=jnp.int32)[None, :]
    m1 = m // a
    m0 = m % a
    k1 = jnp.arange(a, dtype=jnp.int32)[:, None]
    k0 = jnp.arange(b, dtype=jnp.int32)[:, None]
    ar, ai = unit_phase(k1 * m0 % a, a)
    br, bi = unit_phase(k0 * m1 % b, b)
    cr, ci = unit_phase(k0 * m0, length)
    er = br * cr - bi * ci
    ei = br * ci + bi * cr
    plus, minus = lax.optimization_barrier((er + ei, er - ei))
    table = ar[:, None, :] * plus[None] + ai[:, None, :] * minus[None]
    return table.reshape(length, length)


def wave_squared(index, length):
    folded = jnp.minimum(index, length - index).astype(jnp.float32)
    return (folded * (2.0 * jnp.pi / length)) ** 2


def body(concentration, potential, lift, eigenvalue, basis, inverse_basis):
    fast = lax.Precision.HIGH
    both = ("lev", "pln")
    lev_count = lax.axis_size("lev")
    pln_count = lax.axis_size("pln")
    devices = lev_count * pln_count
    flat_index = lax.axis_index("lev") * pln_count + lax.axis_index("pln")
    own_levels, own_rows, width_y = concentration.shape
    width_x = own_rows * pln_count
    cols = width_y // devices
    table_y = lax.optimization_barrier(cas_table(width_y))
    table_x = table_y if width_x == width_y else lax.optimization_barrier(cas_table(width_x))
    table_rx = table_x.reshape(pln_count, own_rows, width_x)

    def forward(planes_in):
        planes = planes_in.shape[0]
        along_y = lax.optimization_barrier(jnp.einsum("lxn,nk->lxk", planes_in, table_y, precision=fast))
        send = along_y.reshape(planes, own_rows, devices, cols).transpose(2, 0, 3, 1)
        send = send.reshape(devices, planes * cols, own_rows)
        recv = lax.all_to_all(send, both, split_axis=0, concat_axis=0, tiled=True)
        recv = recv.reshape(lev_count, pln_count, planes, cols, own_rows)
        return jnp.einsum("aplkx,pxn->alkn", recv, table_rx, precision=fast)

    nonlinear = concentration**3 - concentration
    surface = 2.0 * EXCHANGE_CURRENT * jnp.sinh(0.5 * (potential - concentration[0]))
    second_spectral = forward(nonlinear)
    first_spectral = forward(jnp.concatenate([concentration, surface[None]], axis=0))
    basis_inv = inverse_basis.reshape(inverse_basis.shape[0], lev_count, own_levels)
    lift_weight = jnp.einsum("ml,l->m", inverse_basis, lift, precision=lax.Precision.HIGHEST)
    eigen_first = (
        jnp.einsum("mai,aikn->mkn", basis_inv, first_spectral[:, :own_levels], precision=fast)
        + TIME_STEP * lift_weight[:, None, None] * first_spectral[0, own_levels][None]
    )
    eigen_second = jnp.einsum("mai,aikn->mkn", basis_inv, second_spectral, precision=fast)
    y_index = flat_index * cols + jnp.arange(cols, dtype=jnp.int32)
    x_index = jnp.arange(width_x, dtype=jnp.int32)
    total_wave = wave_squared(y_index, width_y)[:, None] + wave_squared(x_index, width_x)[None, :]
    operator = total_wave[None] + eigenvalue[:, None, None]
    numerator = eigen_first - TIME_STEP * operator * eigen_second
    update = numerator / (1.0 + TIME_STEP * GRADIENT_ENERGY * operator * operator)
    level_values = jnp.einsum("lm,mkn->lkn", basis, update, precision=fast)
    back_x = jnp.einsum("lkn,nx->lkx", level_values, table_x, precision=fast)
    send_b = back_x.reshape(lev_count, own_levels, cols, pln_count, own_rows).transpose(0, 3, 1, 2, 4)
    send_b = send_b.reshape(devices, own_levels * cols, own_rows)
    recv_b = lax.all_to_all(send_b, both, split_axis=0, concat_axis=0, tiled=True)
    recv_b = recv_b.reshape(devices, own_levels, cols, own_rows).transpose(1, 3, 0, 2)
    recv_b = lax.optimization_barrier(recv_b.reshape(own_levels, own_rows, width_y))
    scale_factor = 1.0 / (width_x * width_y)
    return jnp.einsum("ixk,kn->ixn", recv_b, table_y, precision=fast) * scale_factor


def solution(mesh):
    in_specs = (P("lev", "pln", None), P("pln", None), P(), P(), P(), P())
    out_specs = P("lev", "pln", None)
    return jax.shard_map(body, mesh=mesh, in_specs=in_specs, out_specs=out_specs, check_vma=False)
```

```python
import math

import jax
import jax.numpy as jnp
from jax import lax
from jax.sharding import PartitionSpec as P

TIME_STEP = 0.04
GRADIENT_ENERGY = 0.25
EXCHANGE_CURRENT = 0.6


def unit_phase(numerator, denominator):
    angle = numerator.astype(jnp.float32) * (2.0 * jnp.pi / denominator)
    return lax.optimization_barrier((jnp.cos(angle), jnp.sin(angle)))


def cas_table(length):
    b = 1 << (int(math.log2(length)) // 2)
    if length % b:
        index = jnp.arange(length, dtype=jnp.int32)
        cos_part, sin_part = unit_phase(index[:, None] * index[None, :] % length, length)
        return cos_part + sin_part
    a = length // b
    m = jnp.arange(length, dtype=jnp.int32)[None, :]
    m1 = m // a
    m0 = m % a
    k1 = jnp.arange(a, dtype=jnp.int32)[:, None]
    k0 = jnp.arange(b, dtype=jnp.int32)[:, None]
    ar, ai = unit_phase(k1 * m0 % a, a)
    br, bi = unit_phase(k0 * m1 % b, b)
    cr, ci = unit_phase(k0 * m0, length)
    er = br * cr - bi * ci
    ei = br * ci + bi * cr
    plus, minus = lax.optimization_barrier((er + ei, er - ei))
    table = ar[:, None, :] * plus[None] + ai[:, None, :] * minus[None]
    return table.reshape(length, length)


def wave_squared(index, length):
    folded = jnp.minimum(index, length - index).astype(jnp.float32)
    return (folded * (2.0 * jnp.pi / length)) ** 2


def body(concentration, potential, lift, eigenvalue, basis, inverse_basis):
    fast = lax.Precision.HIGH
    both = ("lev", "pln")
    lev_count = lax.axis_size("lev")
    pln_count = lax.axis_size("pln")
    devices = lev_count * pln_count
    flat_index = lax.axis_index("lev") * pln_count + lax.axis_index("pln")
    own_levels, own_rows, width_y = concentration.shape
    width_x = own_rows * pln_count
    cols = width_y // devices
    table_y = lax.optimization_barrier(cas_table(width_y))
    table_x = table_y if width_x == width_y else lax.optimization_barrier(cas_table(width_x))
    table_rx = table_x.reshape(pln_count, own_rows, width_x)

    def forward(planes_in):
        planes = planes_in.shape[0]
        along_y = lax.optimization_barrier(jnp.einsum("lxn,nk->lxk", planes_in, table_y, precision=fast))
        send = along_y.reshape(planes, own_rows, devices, cols).transpose(2, 0, 3, 1)
        send = send.reshape(devices, planes * cols, own_rows)
        recv = lax.all_to_all(send, both, split_axis=0, concat_axis=0, tiled=True)
        recv = recv.reshape(lev_count, pln_count, planes, cols, own_rows)
        return jnp.einsum("aplkx,pxn->alkn", recv, table_rx, precision=fast)

    nonlinear = concentration**3 - concentration
    surface = 2.0 * EXCHANGE_CURRENT * jnp.sinh(0.5 * (potential - concentration[0]))
    split = own_levels // 2
    early = forward(nonlinear[:split])
    late = forward(jnp.concatenate([nonlinear[split:], concentration, surface[None]], axis=0))
    rest = own_levels - split
    second_spectral = jnp.concatenate([early, late[:, :rest]], axis=1)
    first_spectral = late[:, rest:]
    basis_inv = inverse_basis.reshape(inverse_basis.shape[0], lev_count, own_levels)
    lift_weight = jnp.einsum("ml,l->m", inverse_basis, lift, precision=lax.Precision.HIGHEST)
    eigen_first = (
        jnp.einsum("mai,aikn->mkn", basis_inv, first_spectral[:, :own_levels], precision=fast)
        + TIME_STEP * lift_weight[:, None, None] * first_spectral[0, own_levels][None]
    )
    eigen_second = jnp.einsum("mai,aikn->mkn", basis_inv, second_spectral, precision=fast)
    y_index = flat_index * cols + jnp.arange(cols, dtype=jnp.int32)
    x_index = jnp.arange(width_x, dtype=jnp.int32)
    total_wave = wave_squared(y_index, width_y)[:, None] + wave_squared(x_index, width_x)[None, :]
    operator = total_wave[None] + eigenvalue[:, None, None]
    numerator = eigen_first - TIME_STEP * operator * eigen_second
    update = numerator / (1.0 + TIME_STEP * GRADIENT_ENERGY * operator * operator)
    level_values = jnp.einsum("lm,mkn->lkn", basis, update, precision=fast)
    back_x = jnp.einsum("lkn,nx->lkx", level_values, table_x, precision=fast)
    send_b = back_x.reshape(lev_count, own_levels, cols, pln_count, own_rows).transpose(0, 3, 1, 2, 4)
    send_b = send_b.reshape(devices, own_levels * cols, own_rows)
    recv_b = lax.all_to_all(send_b, both, split_axis=0, concat_axis=0, tiled=True)
    recv_b = recv_b.reshape(devices, own_levels, cols, own_rows).transpose(1, 3, 0, 2)
    recv_b = lax.optimization_barrier(recv_b.reshape(own_levels, own_rows, width_y))
    scale_factor = 1.0 / (width_x * width_y)
    return jnp.einsum("ixk,kn->ixn", recv_b, table_y, precision=fast) * scale_factor


def solution(mesh):
    in_specs = (P("lev", "pln", None), P("pln", None), P(), P(), P(), P())
    out_specs = P("lev", "pln", None)
    return jax.shard_map(body, mesh=mesh, in_specs=in_specs, out_specs=out_specs, check_vma=False)
```

```python
import math

import jax
import jax.numpy as jnp
from jax import lax
from jax.sharding import PartitionSpec as P

TIME_STEP = 0.04
GRADIENT_ENERGY = 0.25
EXCHANGE_CURRENT = 0.6


def unit_phase(numerator, denominator):
    angle = numerator.astype(jnp.float32) * (2.0 * jnp.pi / denominator)
    return lax.optimization_barrier((jnp.cos(angle), jnp.sin(angle)))


def cas_table(length):
    b = 1 << (int(math.log2(length)) // 2)
    if length % b:
        index = jnp.arange(length, dtype=jnp.int32)
        cos_part, sin_part = unit_phase(index[:, None] * index[None, :] % length, length)
        return cos_part + sin_part
    a = length // b
    m = jnp.arange(length, dtype=jnp.int32)[None, :]
    m1 = m // a
    m0 = m % a
    k1 = jnp.arange(a, dtype=jnp.int32)[:, None]
    k0 = jnp.arange(b, dtype=jnp.int32)[:, None]
    ar, ai = unit_phase(k1 * m0 % a, a)
    br, bi = unit_phase(k0 * m1 % b, b)
    cr, ci = unit_phase(k0 * m0, length)
    er = br * cr - bi * ci
    ei = br * ci + bi * cr
    plus, minus = lax.optimization_barrier((er + ei, er - ei))
    table = ar[:, None, :] * plus[None] + ai[:, None, :] * minus[None]
    return table.reshape(length, length)


def wave_squared(index, length):
    folded = jnp.minimum(index, length - index).astype(jnp.float32)
    return (folded * (2.0 * jnp.pi / length)) ** 2


def body(concentration, potential, lift, eigenvalue, basis, inverse_basis):
    fast = lax.Precision.HIGH
    both = ("lev", "pln")
    lev_count = lax.axis_size("lev")
    pln_count = lax.axis_size("pln")
    devices = lev_count * pln_count
    flat_index = lax.axis_index("lev") * pln_count + lax.axis_index("pln")
    own_levels, own_rows, width_y = concentration.shape
    width_x = own_rows * pln_count
    cols = width_y // devices
    table_y = lax.optimization_barrier(cas_table(width_y))
    table_x = table_y if width_x == width_y else lax.optimization_barrier(cas_table(width_x))
    table_rx = table_x.reshape(pln_count, own_rows, width_x)

    def forward(planes_in):
        planes = planes_in.shape[0]
        along_y = lax.optimization_barrier(jnp.einsum("lxn,nk->lxk", planes_in, table_y, precision=fast))
        send = along_y.reshape(planes, own_rows, devices, cols).transpose(2, 0, 3, 1)
        send = send.reshape(devices, planes * cols, own_rows)
        recv = lax.all_to_all(send, both, split_axis=0, concat_axis=0, tiled=True)
        recv = recv.reshape(lev_count, pln_count, planes, cols, own_rows)
        return jnp.einsum("aplkx,pxn->alkn", recv, table_rx, precision=fast)

    nonlinear = concentration**3 - concentration
    surface = 2.0 * EXCHANGE_CURRENT * jnp.sinh(0.5 * (potential - concentration[0]))
    surface_spectral = forward(surface[None])
    fields = forward(jnp.concatenate([concentration, nonlinear], axis=0))
    first_spectral = jnp.concatenate([fields[:, :own_levels], surface_spectral], axis=1)
    second_spectral = fields[:, own_levels:]
    basis_inv = inverse_basis.reshape(inverse_basis.shape[0], lev_count, own_levels)
    lift_weight = jnp.einsum("ml,l->m", inverse_basis, lift, precision=lax.Precision.HIGHEST)
    eigen_first = (
        jnp.einsum("mai,aikn->mkn", basis_inv, first_spectral[:, :own_levels], precision=fast)
        + TIME_STEP * lift_weight[:, None, None] * first_spectral[0, own_levels][None]
    )
    eigen_second = jnp.einsum("mai,aikn->mkn", basis_inv, second_spectral, precision=fast)
    y_index = flat_index * cols + jnp.arange(cols, dtype=jnp.int32)
    x_index = jnp.arange(width_x, dtype=jnp.int32)
    total_wave = wave_squared(y_index, width_y)[:, None] + wave_squared(x_index, width_x)[None, :]
    operator = total_wave[None] + eigenvalue[:, None, None]
    numerator = eigen_first - TIME_STEP * operator * eigen_second
    update = numerator / (1.0 + TIME_STEP * GRADIENT_ENERGY * operator * operator)
    level_values = jnp.einsum("lm,mkn->lkn", basis, update, precision=fast)
    back_x = jnp.einsum("lkn,nx->lkx", level_values, table_x, precision=fast)
    send_b = back_x.reshape(lev_count, own_levels, cols, pln_count, own_rows).transpose(0, 3, 1, 2, 4)
    send_b = send_b.reshape(devices, own_levels * cols, own_rows)
    recv_b = lax.all_to_all(send_b, both, split_axis=0, concat_axis=0, tiled=True)
    recv_b = recv_b.reshape(devices, own_levels, cols, own_rows).transpose(1, 3, 0, 2)
    recv_b = lax.optimization_barrier(recv_b.reshape(own_levels, own_rows, width_y))
    scale_factor = 1.0 / (width_x * width_y)
    return jnp.einsum("ixk,kn->ixn", recv_b, table_y, precision=fast) * scale_factor


def solution(mesh):
    in_specs = (P("lev", "pln", None), P("pln", None), P(), P(), P(), P())
    out_specs = P("lev", "pln", None)
    return jax.shard_map(body, mesh=mesh, in_specs=in_specs, out_specs=out_specs, check_vma=False)
```

```python
import math

import jax
import jax.numpy as jnp
from jax import lax
from jax.sharding import PartitionSpec as P

TIME_STEP = 0.04
GRADIENT_ENERGY = 0.25
EXCHANGE_CURRENT = 0.6


def unit_phase(numerator, denominator):
    angle = numerator.astype(jnp.float32) * (2.0 * jnp.pi / denominator)
    return lax.optimization_barrier((jnp.cos(angle), jnp.sin(angle)))


def cas_table(length):
    b = 1 << (int(math.log2(length)) // 2)
    if length % b:
        index = jnp.arange(length, dtype=jnp.int32)
        cos_part, sin_part = unit_phase(index[:, None] * index[None, :] % length, length)
        return cos_part + sin_part
    a = length // b
    m = jnp.arange(length, dtype=jnp.int32)[None, :]
    m1 = m // a
    m0 = m % a
    k1 = jnp.arange(a, dtype=jnp.int32)[:, None]
    k0 = jnp.arange(b, dtype=jnp.int32)[:, None]
    ar, ai = unit_phase(k1 * m0 % a, a)
    br, bi = unit_phase(k0 * m1 % b, b)
    cr, ci = unit_phase(k0 * m0, length)
    er = br * cr - bi * ci
    ei = br * ci + bi * cr
    plus, minus = lax.optimization_barrier((er + ei, er - ei))
    table = ar[:, None, :] * plus[None] + ai[:, None, :] * minus[None]
    return table.reshape(length, length)


def wave_squared(index, length):
    folded = jnp.minimum(index, length - index).astype(jnp.float32)
    return (folded * (2.0 * jnp.pi / length)) ** 2


def body(concentration, potential, lift, eigenvalue, basis, inverse_basis):
    highest = lax.Precision.HIGHEST
    fast = lax.Precision.HIGH
    both = ("lev", "pln")
    lev_count = lax.axis_size("lev")
    pln_count = lax.axis_size("pln")
    devices = lev_count * pln_count
    flat_index = lax.axis_index("lev") * pln_count + lax.axis_index("pln")
    own_levels, own_rows, width_y = concentration.shape
    width_x = own_rows * pln_count
    cols = width_y // devices
    table_y = lax.optimization_barrier(cas_table(width_y))
    table_x = table_y if width_x == width_y else lax.optimization_barrier(cas_table(width_x))
    table_rx = table_x.reshape(pln_count, own_rows, width_x)

    def forward(planes_in):
        planes = planes_in.shape[0]
        along_y = lax.optimization_barrier(jnp.einsum("lxn,nk->lxk", planes_in, table_y, precision=fast))
        send = along_y.reshape(planes, own_rows, devices, cols).transpose(2, 0, 3, 1)
        send = send.reshape(devices, planes * cols, own_rows)
        recv = lax.all_to_all(send, both, split_axis=0, concat_axis=0, tiled=True)
        recv = recv.reshape(lev_count, pln_count, planes, cols, own_rows)
        return jnp.einsum("aplkx,pxn->alkn", recv, table_rx, precision=fast)

    nonlinear = concentration**3 - concentration
    surface = 2.0 * EXCHANGE_CURRENT * jnp.sinh(0.5 * (potential - concentration[0]))
    split = own_levels // 2
    early = forward(nonlinear[:split])
    late = forward(jnp.concatenate([nonlinear[split:], concentration, surface[None]], axis=0))
    rest = own_levels - split
    second_spectral = jnp.concatenate([early, late[:, :rest]], axis=1)
    first_spectral = late[:, rest:]
    basis_inv = inverse_basis.reshape(inverse_basis.shape[0], lev_count, own_levels)
    lift_weight = jnp.einsum("ml,l->m", inverse_basis, lift, precision=highest)
    eigen_first = (
        jnp.einsum("mai,aikn->mkn", basis_inv, first_spectral[:, :own_levels], precision=highest)
        + TIME_STEP * lift_weight[:, None, None] * first_spectral[0, own_levels][None]
    )
    eigen_second = jnp.einsum("mai,aikn->mkn", basis_inv, second_spectral, precision=highest)
    y_index = flat_index * cols + jnp.arange(cols, dtype=jnp.int32)
    x_index = jnp.arange(width_x, dtype=jnp.int32)
    total_wave = wave_squared(y_index, width_y)[:, None] + wave_squared(x_index, width_x)[None, :]
    operator = total_wave[None] + eigenvalue[:, None, None]
    numerator = eigen_first - TIME_STEP * operator * eigen_second
    update = numerator / (1.0 + TIME_STEP * GRADIENT_ENERGY * operator * operator)
    level_values = jnp.einsum("lm,mkn->lkn", basis, update, precision=highest)
    back_x = jnp.einsum("lkn,nx->lkx", level_values, table_x, precision=fast)
    send_b = back_x.reshape(lev_count, own_levels, cols, pln_count, own_rows).transpose(0, 3, 1, 2, 4)
    send_b = send_b.reshape(devices, own_levels * cols, own_rows)
    recv_b = lax.all_to_all(send_b, both, split_axis=0, concat_axis=0, tiled=True)
    recv_b = recv_b.reshape(devices, own_levels, cols, own_rows).transpose(1, 3, 0, 2)
    recv_b = lax.optimization_barrier(recv_b.reshape(own_levels, own_rows, width_y))
    scale_factor = 1.0 / (width_x * width_y)
    return jnp.einsum("ixk,kn->ixn", recv_b, table_y, precision=fast) * scale_factor


def solution(mesh):
    in_specs = (P("lev", "pln", None), P("pln", None), P(), P(), P(), P())
    out_specs = P("lev", "pln", None)
    return jax.shard_map(body, mesh=mesh, in_specs=in_specs, out_specs=out_specs, check_vma=False)
```

```python
import math

import jax
import jax.numpy as jnp
from jax import lax
from jax.sharding import PartitionSpec as P

TIME_STEP = 0.04
GRADIENT_ENERGY = 0.25
EXCHANGE_CURRENT = 0.6


def unit_phase(numerator, denominator):
    angle = numerator.astype(jnp.float32) * (2.0 * jnp.pi / denominator)
    return lax.optimization_barrier((jnp.cos(angle), jnp.sin(angle)))


def cas_table(length):
    b = 1 << (int(math.log2(length)) // 2)
    if length % b:
        index = jnp.arange(length, dtype=jnp.int32)
        cos_part, sin_part = unit_phase(index[:, None] * index[None, :] % length, length)
        return cos_part + sin_part
    a = length // b
    m = jnp.arange(length, dtype=jnp.int32)[None, :]
    m1 = m // a
    m0 = m % a
    k1 = jnp.arange(a, dtype=jnp.int32)[:, None]
    k0 = jnp.arange(b, dtype=jnp.int32)[:, None]
    ar, ai = unit_phase(k1 * m0 % a, a)
    br, bi = unit_phase(k0 * m1 % b, b)
    cr, ci = unit_phase(k0 * m0, length)
    er = br * cr - bi * ci
    ei = br * ci + bi * cr
    plus, minus = lax.optimization_barrier((er + ei, er - ei))
    table = ar[:, None, :] * plus[None] + ai[:, None, :] * minus[None]
    return table.reshape(length, length)


def wave_squared(index, length):
    folded = jnp.minimum(index, length - index).astype(jnp.float32)
    return (folded * (2.0 * jnp.pi / length)) ** 2


def body(concentration, potential, lift, eigenvalue, basis, inverse_basis):
    highest = lax.Precision.HIGHEST
    fast = lax.Precision.HIGH
    both = ("lev", "pln")
    lev_count = lax.axis_size("lev")
    pln_count = lax.axis_size("pln")
    devices = lev_count * pln_count
    flat_index = lax.axis_index("lev") * pln_count + lax.axis_index("pln")
    own_levels, own_rows, width_y = concentration.shape
    width_x = own_rows * pln_count
    cols = width_y // devices
    table_y = lax.optimization_barrier(cas_table(width_y))
    table_x = table_y if width_x == width_y else lax.optimization_barrier(cas_table(width_x))
    table_rx = table_x.reshape(pln_count, own_rows, width_x)

    def forward(planes_in, keep_natural):
        planes = planes_in.shape[0]
        along_y = jnp.einsum("lxn,nk->lxk", planes_in, table_y, precision=fast)
        if keep_natural:
            along_y = lax.optimization_barrier(along_y)
        send = along_y.reshape(planes, own_rows, devices, cols).transpose(2, 0, 3, 1)
        send = send.reshape(devices, planes * cols, own_rows)
        recv = lax.all_to_all(send, both, split_axis=0, concat_axis=0, tiled=True)
        recv = recv.reshape(lev_count, pln_count, planes, cols, own_rows)
        return jnp.einsum("aplkx,pxn->alkn", recv, table_rx, precision=fast)

    nonlinear = concentration**3 - concentration
    surface = 2.0 * EXCHANGE_CURRENT * jnp.sinh(0.5 * (potential - concentration[0]))
    split = own_levels // 2
    early = forward(nonlinear[:split], False)
    late = forward(jnp.concatenate([nonlinear[split:], concentration, surface[None]], axis=0), True)
    rest = own_levels - split
    second_spectral = jnp.concatenate([early, late[:, :rest]], axis=1)
    first_spectral = late[:, rest:]
    basis_inv = inverse_basis.reshape(inverse_basis.shape[0], lev_count, own_levels)
    lift_weight = jnp.einsum("ml,l->m", inverse_basis, lift, precision=highest)
    eigen_first = (
        jnp.einsum("mai,aikn->mkn", basis_inv, first_spectral[:, :own_levels], precision=highest)
        + TIME_STEP * lift_weight[:, None, None] * first_spectral[0, own_levels][None]
    )
    eigen_second = jnp.einsum("mai,aikn->mkn", basis_inv, second_spectral, precision=highest)
    y_index = flat_index * cols + jnp.arange(cols, dtype=jnp.int32)
    x_index = jnp.arange(width_x, dtype=jnp.int32)
    total_wave = wave_squared(y_index, width_y)[:, None] + wave_squared(x_index, width_x)[None, :]
    operator = total_wave[None] + eigenvalue[:, None, None]
    numerator = eigen_first - TIME_STEP * operator * eigen_second
    update = numerator / (1.0 + TIME_STEP * GRADIENT_ENERGY * operator * operator)
    level_values = jnp.einsum("lm,mkn->lkn", basis, update, precision=highest)
    back_x = jnp.einsum("lkn,nx->lkx", level_values, table_x, precision=fast)
    send_b = back_x.reshape(lev_count, own_levels, cols, pln_count, own_rows).transpose(0, 3, 1, 2, 4)
    send_b = send_b.reshape(devices, own_levels * cols, own_rows)
    recv_b = lax.all_to_all(send_b, both, split_axis=0, concat_axis=0, tiled=True)
    recv_b = recv_b.reshape(devices, own_levels, cols, own_rows).transpose(1, 3, 0, 2)
    recv_b = lax.optimization_barrier(recv_b.reshape(own_levels, own_rows, width_y))
    scale_factor = 1.0 / (width_x * width_y)
    return jnp.einsum("ixk,kn->ixn", recv_b, table_y, precision=fast) * scale_factor


def solution(mesh):
    in_specs = (P("lev", "pln", None), P("pln", None), P(), P(), P(), P())
    out_specs = P("lev", "pln", None)
    return jax.shard_map(body, mesh=mesh, in_specs=in_specs, out_specs=out_specs, check_vma=False)
```

```python
import math

import jax
import jax.numpy as jnp
from jax import lax
from jax.sharding import PartitionSpec as P

TIME_STEP = 0.04
GRADIENT_ENERGY = 0.25
EXCHANGE_CURRENT = 0.6


def unit_phase(numerator, denominator):
    angle = numerator.astype(jnp.float32) * (2.0 * jnp.pi / denominator)
    return lax.optimization_barrier((jnp.cos(angle), jnp.sin(angle)))


def cas_table(length):
    b = 1 << (int(math.log2(length)) // 2)
    if length % b:
        index = jnp.arange(length, dtype=jnp.int32)
        cos_part, sin_part = unit_phase(index[:, None] * index[None, :] % length, length)
        return cos_part + sin_part
    a = length // b
    m = jnp.arange(length, dtype=jnp.int32)[None, :]
    m1 = m // a
    m0 = m % a
    k1 = jnp.arange(a, dtype=jnp.int32)[:, None]
    k0 = jnp.arange(b, dtype=jnp.int32)[:, None]
    ar, ai = unit_phase(k1 * m0 % a, a)
    br, bi = unit_phase(k0 * m1 % b, b)
    cr, ci = unit_phase(k0 * m0, length)
    er = br * cr - bi * ci
    ei = br * ci + bi * cr
    plus, minus = lax.optimization_barrier((er + ei, er - ei))
    table = ar[:, None, :] * plus[None] + ai[:, None, :] * minus[None]
    return table.reshape(length, length)


def wave_squared(index, length):
    folded = jnp.minimum(index, length - index).astype(jnp.float32)
    return (folded * (2.0 * jnp.pi / length)) ** 2


def body(concentration, potential, lift, eigenvalue, basis, inverse_basis):
    highest = lax.Precision.HIGHEST
    fast = lax.Precision.HIGH
    both = ("lev", "pln")
    lev_count = lax.axis_size("lev")
    pln_count = lax.axis_size("pln")
    devices = lev_count * pln_count
    flat_index = lax.axis_index("lev") * pln_count + lax.axis_index("pln")
    own_levels, own_rows, width_y = concentration.shape
    width_x = own_rows * pln_count
    cols = width_y // devices
    table_y = lax.optimization_barrier(cas_table(width_y))
    table_x = table_y if width_x == width_y else lax.optimization_barrier(cas_table(width_x))
    table_rx = table_x.reshape(pln_count, own_rows, width_x)

    def forward(planes_in, keep_natural):
        planes = planes_in.shape[0]
        along_y = jnp.einsum("lxn,nk->lxk", planes_in, table_y, precision=fast)
        if keep_natural:
            along_y = lax.optimization_barrier(along_y)
        send = along_y.reshape(planes, own_rows, devices, cols).transpose(2, 0, 3, 1)
        send = send.reshape(devices, planes * cols, own_rows)
        recv = lax.all_to_all(send, both, split_axis=0, concat_axis=0, tiled=True)
        recv = recv.reshape(lev_count, pln_count, planes, cols, own_rows)
        return jnp.einsum("aplkx,pxn->alkn", recv, table_rx, precision=fast)

    nonlinear = concentration**3 - concentration
    surface = 2.0 * EXCHANGE_CURRENT * jnp.sinh(0.5 * (potential - concentration[0]))
    split = own_levels // 2
    early = forward(nonlinear[:split], False)
    late = forward(jnp.concatenate([nonlinear[split:], concentration, surface[None]], axis=0), True)
    rest = own_levels - split
    first_spectral = late[:, rest:]
    basis_inv = inverse_basis.reshape(inverse_basis.shape[0], lev_count, own_levels)
    lift_weight = jnp.einsum("ml,l->m", inverse_basis, lift, precision=highest)
    eigen_first = (
        jnp.einsum("mai,aikn->mkn", basis_inv, first_spectral[:, :own_levels], precision=highest)
        + TIME_STEP * lift_weight[:, None, None] * first_spectral[0, own_levels][None]
    )
    eigen_second = jnp.einsum(
        "mai,aikn->mkn", basis_inv[:, :, :split], early, precision=highest
    ) + jnp.einsum("mai,aikn->mkn", basis_inv[:, :, split:], late[:, :rest], precision=highest)
    y_index = flat_index * cols + jnp.arange(cols, dtype=jnp.int32)
    x_index = jnp.arange(width_x, dtype=jnp.int32)
    total_wave = wave_squared(y_index, width_y)[:, None] + wave_squared(x_index, width_x)[None, :]
    operator = total_wave[None] + eigenvalue[:, None, None]
    numerator = eigen_first - TIME_STEP * operator * eigen_second
    update = numerator / (1.0 + TIME_STEP * GRADIENT_ENERGY * operator * operator)
    level_values = jnp.einsum("lm,mkn->lkn", basis, update, precision=highest)
    back_x = jnp.einsum("lkn,nx->lkx", level_values, table_x, precision=fast)
    send_b = back_x.reshape(lev_count, own_levels, cols, pln_count, own_rows).transpose(0, 3, 1, 2, 4)
    send_b = send_b.reshape(devices, own_levels * cols, own_rows)
    recv_b = lax.all_to_all(send_b, both, split_axis=0, concat_axis=0, tiled=True)
    recv_b = recv_b.reshape(devices, own_levels, cols, own_rows).transpose(1, 3, 0, 2)
    recv_b = lax.optimization_barrier(recv_b.reshape(own_levels, own_rows, width_y))
    scale_factor = 1.0 / (width_x * width_y)
    return jnp.einsum("ixk,kn->ixn", recv_b, table_y, precision=fast) * scale_factor


def solution(mesh):
    in_specs = (P("lev", "pln", None), P("pln", None), P(), P(), P(), P())
    out_specs = P("lev", "pln", None)
    return jax.shard_map(body, mesh=mesh, in_specs=in_specs, out_specs=out_specs, check_vma=False)
```
